128 devices in a mesh: lon: 16 (over x_hi, z, core), lat: 8 (over x_lo, y).
Axes of the slice: x: 4 (x_hi: 2, x_lo: 2; x = x_hi * 2 + x_lo), y: 4, z: 4, core: 2. Of those that a mesh axis runs over, the one named last changes fastest.
Arguments:
- ensemble_prediction: bfloat16 [408, 512, 4096], P(None, 'lat', 'lon'), may hold values from -6 to 6
- mapping_matrix: bfloat16 [96, 408], replicated, may hold values from -0.3125 to 0.3125
- mapping_offset: float32 [96], replicated, may hold values from -3 to 3
- gauge_measured_records: bfloat16 [524288, 256], P(('lon', 'lat')), may hold values from -6 to 6
- gauge_scatter_matrix: bfloat16 [256, 96], replicated, may hold values from -0.375 to 0.375
- gauge_scatter_offset: float32 [96], replicated, may hold values from -3 to 3
- gauge_block_number: int32 [524288, 1], P(('lon', 'lat')), may hold values from 0 to 127; in each aligned block of 4096 rows (0 to 4095, 4096 to 8191, ...) at most 64 rows name the same one
- gauge_point_position: int32 [524288], P(('lon', 'lat')), may hold values from 0 to 16383
- initial_filter_matrix: bfloat16 [96, 96, 3, 3], replicated, may hold values from -0.21875 to 0.21875
- initial_filter_offset: float32 [96], replicated, may hold values from -3 to 3
- latter_filter_matrix: bfloat16 [96, 96, 3, 3], replicated, may hold values from -0.21875 to 0.21875
- latter_filter_offset: float32 [96], replicated, may hold values from -3 to 3
Outputs:
- corrected: bfloat16 [96, 512, 4096], P(None, 'lat', 'lon')
- station_values: bfloat16 [524288, 96], P(('lon', 'lat'))
The draws below stay inside these ranges and needn't reach their ends.
Inputs may be any that keep to these rules, and one draw needn't show every extreme that they name: `gauge_block_number`: among the 4096 rows of one device, at most 64 name the same tile, a bound that some block reaches.
All inputs are finite; a program needn't handle non-finite values.
Results may differ from the reference program's by a relative error of at most 0.01.
Values may be sent and summed in bfloat16 or wider, within the bound.
No kernel may reach another device: no remote copies, remote signals or barrier semaphores. Data moves between devices by JAX's collectives and lax.ppermute only.
A program may use at most 192 MiB of HBM per device.

```python
import math
import jax
import jax.numpy as jnp
import numpy as np
from jax import lax

FEATURE_DEPTH = 408
F = 96
OBS = 256
LATC = 64
LONC = 256
STA_DEV = 4096
NORTH_SOUTH_SPAN = 512
EAST_WEST_SPAN = 4096
S = 524288
CAP = 64
N_LAT = 8
DEVICES = 128


def with_ends(entries, stream_key, least, top_value):
    spot = [jax.random.randint(jax.random.fold_in(stream_key, axis), (), 0, length) for axis, length in enumerate(entries.shape)]
    widest = entries.shape.index(max(entries.shape))
    neighbour = spot[:widest] + [(spot[widest] + 1) % entries.shape[widest]] + spot[widest + 1:]
    return entries.at[tuple(spot)].set(least).at[tuple(neighbour)].set(top_value)


def steps_of(own_key, dims, cuts, least, high):
    gain, own = 1.0, jax.random.fold_in(own_key, 6)
    for dim, shards_of in cuts:
        heights = jnp.exp(jax.random.uniform(jax.random.fold_in(own, dim), (shards_of,), jnp.float32, least / len(cuts), high / len(cuts)))
        gain = gain * jnp.repeat(heights, dims[dim] // shards_of).reshape([-1 if axis == dim else 1 for axis in range(len(dims))])
    return gain


def assign_block(rng, own, number, rows, number_of, top, reach, skew):
    order = jax.random.permutation(rng, number_of)
    crowded, usual = load_shares(number_of, rows * top, reach, skew, True), load_shares(number_of, rows * top, reach, skew, False)
    places = jnp.arange(number_of)

    def named(lengths, offset_by):
        used = int((lengths > 0).sum())
        fixed = max(1, used // 4)
        moved = fixed + (places - fixed + offset_by * (used - fixed)) % max(1, number_of - fixed)
        return jnp.zeros((number_of,), jnp.int32).at[order[jnp.where(places < fixed, places, moved)]].set(jnp.asarray(lengths, jnp.int32))

    lengths = jnp.where(number % 4 == 0, named(crowded, number // 4), named(usual, number - number // 4 - 1))
    mixed = jax.random.permutation(jax.random.fold_in(own, 3), number_of)
    giver, sink = mixed[0:number_of // 2 * 2:2], mixed[1:number_of // 2 * 2:2]
    room = jnp.minimum(lengths[giver] - 1, reach - lengths[sink]) // 2
    room = jnp.where((giver == order[0]) | (sink == order[0]) | (lengths[sink] == 0), 0, jnp.maximum(room, 0))
    moved = jax.random.randint(jax.random.fold_in(own, 4), (number_of // 2,), 0, 1 << 20) % (room + 1)
    lengths = lengths.at[giver].add(-moved).at[sink].add(moved)
    items = jnp.searchsorted(jnp.cumsum(lengths), jnp.arange(rows * top), side="right").astype(jnp.int32)
    listing = items.reshape(top, rows).T
    listing = listing[jax.random.permutation(jax.random.fold_in(own, 1), rows)]
    offset_by = jax.random.randint(jax.random.fold_in(own, 2), (rows, 1), 0, top)
    return jnp.take_along_axis(listing, (jnp.arange(top)[None, :] + offset_by) % top, axis=1)


def load_shares(amount, total, bound, slope, full):
    portions = [(1 << 20) // math.isqrt(grade ** slope) + 1 for grade in range(1, amount + 1)]
    largest = bound if full else min(bound, max(-(-total // amount), total * portions[0] // sum(portions)))
    least = 1 if total - largest >= amount - 1 else 0
    given, surplus = [largest] + [least] * (amount - 1), total - largest - least * (amount - 1)
    while surplus > 0:
        movable = [i for i in range(1, amount) if given[i] < largest] or [i for i in range(1, amount) if given[i] < bound]
        mass, left = sum([portions[i] for i in movable]), surplus
        for i in movable:
            extra = min(bound - given[i], max(1, left * portions[i] // mass), surplus)
            given[i] = given[i] + extra
            surplus = surplus - extra
    return np.array(given)


def scatter_about(key, extent, width, reach, pieces=(), kind=jnp.bfloat16):
    array = width * jax.random.normal(key, extent, jnp.float32)
    if pieces:
        array = array * steps_of(key, extent, pieces, -0.22, 0.18)
    return jnp.clip(array, -reach, reach).astype(kind)


def setup_inputs(seed: int = 0) -> dict:
    streams_of = jax.random.split(jax.random.key(seed), 13)
    ensemble_prediction = scatter_about(streams_of[0], (FEATURE_DEPTH, NORTH_SOUTH_SPAN, EAST_WEST_SPAN), 1.0, 6.0, ((1, 8), (2, 16)))
    mapping_matrix = scatter_about(streams_of[1], (F, FEATURE_DEPTH), FEATURE_DEPTH ** -0.5, 0.3125)
    mapping_offset = scatter_about(streams_of[2], (F,), 0.5, 3.0, (), jnp.float32)
    gauge_measured_records = scatter_about(streams_of[3], (S, OBS), 1.0, 6.0, ((0, 128),))
    gauge_scatter_matrix = scatter_about(streams_of[4], (OBS, F), OBS ** -0.5, 0.375)
    gauge_scatter_offset = scatter_about(streams_of[5], (F,), 0.5, 3.0, (), jnp.float32)
    gauge_block_number_keys = jax.random.split(jax.random.fold_in(streams_of[6], 1), S // STA_DEV)
    gauge_block_number_turns = jax.random.permutation(jax.random.fold_in(streams_of[6], 3), S // STA_DEV)
    gauge_block_number = jax.vmap(lambda own, number: assign_block(jax.random.fold_in(streams_of[6], 2), own, number, STA_DEV, DEVICES, 1, CAP, 2))(gauge_block_number_keys, gauge_block_number_turns).reshape((S, 1))
    gauge_point_position = with_ends(jax.random.randint(streams_of[7], (S,), 0, LATC * LONC), jax.random.fold_in(streams_of[7], 1), 0, (LATC * LONC) - 1).astype(jnp.int32)
    initial_filter_matrix = scatter_about(streams_of[8], (F, F, 3, 3), (9 * F) ** -0.5, 0.21875)
    initial_filter_offset = scatter_about(streams_of[9], (F,), 0.5, 3.0, (), jnp.float32)
    latter_filter_matrix = scatter_about(streams_of[10], (F, F, 3, 3), (9 * F) ** -0.5, 0.21875)
    latter_filter_offset = scatter_about(streams_of[11], (F,), 0.5, 3.0, (), jnp.float32)
    return dict(ensemble_prediction=ensemble_prediction, mapping_matrix=mapping_matrix, mapping_offset=mapping_offset, gauge_measured_records=gauge_measured_records, gauge_scatter_matrix=gauge_scatter_matrix, gauge_scatter_offset=gauge_scatter_offset, gauge_block_number=gauge_block_number, gauge_point_position=gauge_point_position, initial_filter_matrix=initial_filter_matrix, initial_filter_offset=initial_filter_offset, latter_filter_matrix=latter_filter_matrix, latter_filter_offset=latter_filter_offset)


def conv_periodic(field, kernel):
    widened = jnp.concatenate([field[:, :, -1:], field, field[:, :, :1]], axis=2)
    widened = jnp.pad(widened, ((0, 0), (1, 1), (0, 0)))
    result = lax.conv_general_dilated(widened.astype(jnp.float32)[None], kernel.astype(jnp.float32), (1, 1), "VALID", dimension_numbers=("NCHW", "OIHW", "NCHW"), precision=lax.Precision.HIGHEST)
    return result[0]


def reference(ensemble_prediction, mapping_matrix, mapping_offset, gauge_measured_records, gauge_scatter_matrix, gauge_scatter_offset, gauge_block_number, gauge_point_position, initial_filter_matrix, initial_filter_offset, latter_filter_matrix, latter_filter_offset):
    mapped_features = jnp.dot(mapping_matrix, ensemble_prediction.reshape(FEATURE_DEPTH, NORTH_SOUTH_SPAN * EAST_WEST_SPAN), preferred_element_type=jnp.float32)
    mapped_features = mapped_features + mapping_offset.astype(jnp.float32)[:, None]
    embedded = (jnp.dot(gauge_measured_records, gauge_scatter_matrix, preferred_element_type=jnp.float32) + gauge_scatter_offset.astype(jnp.float32)[None, :]).astype(jnp.bfloat16)
    tile_index = gauge_block_number[:, 0].astype(jnp.int32)
    lon_index = tile_index // N_LAT
    lat_index = tile_index % N_LAT
    grid_row = lat_index * LATC + gauge_point_position // LONC
    grid_col = lon_index * LONC + gauge_point_position % LONC
    global_cell = (grid_row * EAST_WEST_SPAN + grid_col).astype(jnp.int32)
    merged_sum = mapped_features.at[:, global_cell].add(embedded.astype(jnp.float32).T)
    merged = merged_sum.astype(jnp.bfloat16).reshape(F, NORTH_SOUTH_SPAN, EAST_WEST_SPAN)
    hidden = jax.nn.gelu(conv_periodic(merged, initial_filter_matrix) + initial_filter_offset.astype(jnp.float32)[:, None, None]).astype(jnp.bfloat16)
    corrected = (merged.astype(jnp.float32) + conv_periodic(hidden, latter_filter_matrix) + latter_filter_offset.astype(jnp.float32)[:, None, None]).astype(jnp.bfloat16)
    station_values = corrected.reshape(F, NORTH_SOUTH_SPAN * EAST_WEST_SPAN)[:, global_cell].T
    return corrected, station_values
```

```python
import jax
import jax.numpy as jnp
from jax import lax
from jax.sharding import PartitionSpec as P


def shifted(block, axis, dim, width, periodic):
    count = lax.axis_size(axis)
    forward = [(i, i + 1) for i in range(count - 1)]
    if periodic:
        forward.append((count - 1, 0))
    backward = [(target, source) for source, target in forward]
    low = lax.ppermute(lax.slice_in_dim(block, block.shape[dim] - width, None, axis=dim), axis, forward)
    high = lax.ppermute(lax.slice_in_dim(block, 0, width, axis=dim), axis, backward)
    return jnp.concatenate([low, block, high], axis=dim)


def conv_valid(field, kernel):
    result = lax.conv_general_dilated(
        field[None],
        kernel,
        (1, 1),
        "VALID",
        dimension_numbers=("NCHW", "OIHW", "NCHW"),
        preferred_element_type=jnp.float32,
    )
    return result[0]


def on_device(
    ensemble_prediction,
    mapping_matrix,
    mapping_offset,
    gauge_measured_records,
    gauge_scatter_matrix,
    gauge_scatter_offset,
    gauge_block_number,
    gauge_point_position,
    initial_filter_matrix,
    initial_filter_offset,
    latter_filter_matrix,
    latter_filter_offset,
):
    feature_depth_total, north_south_total, east_west_total = ensemble_prediction.shape
    features = mapping_matrix.shape[0]
    mesh_point_total = north_south_total * east_west_total
    lon_size = lax.axis_size("lon")
    lat_size = lax.axis_size("lat")
    devices = lon_size * lat_size
    held_rows = gauge_measured_records.shape[0]
    capacity = 2 * held_rows // devices
    slot_total = devices * capacity
    target_tile = gauge_block_number[:, 0]
    one_hot = (target_tile[:, None] == jnp.arange(devices, dtype=jnp.int32)[None, :]).astype(
        jnp.int32
    )
    earlier = jnp.cumsum(one_hot, axis=0) - one_hot
    slot_index = jnp.sum(earlier * one_hot, axis=1)
    position = target_tile * capacity + slot_index
    local_embedded = (
        jnp.dot(gauge_measured_records, gauge_scatter_matrix, preferred_element_type=jnp.float32)
        + gauge_scatter_offset[None, :]
    ).astype(jnp.bfloat16)
    cell_row = gauge_point_position // east_west_total
    cell_col = gauge_point_position % east_west_total
    tagged = jnp.concatenate(
        [
            local_embedded,
            (cell_row + 1).astype(jnp.bfloat16)[:, None],
            cell_col.astype(jnp.bfloat16)[:, None],
        ],
        axis=1,
    )
    width = tagged.shape[1]
    payload = jnp.zeros((slot_total, width), jnp.bfloat16).at[position].set(tagged)
    arrived = lax.all_to_all(
        payload.reshape(devices, capacity, width),
        ("lon", "lat"),
        split_axis=0,
        concat_axis=0,
        tiled=True,
    ).reshape(slot_total, width)
    arrived_row = arrived[:, features].astype(jnp.int32) - 1
    arrived_col = arrived[:, features + 1].astype(jnp.int32)
    filled = arrived_row >= 0
    arrived_cells = jnp.where(filled, arrived_row * east_west_total + arrived_col, mesh_point_total)
    mapped_features = (
        jnp.dot(
            mapping_matrix,
            ensemble_prediction.reshape(feature_depth_total, mesh_point_total),
            preferred_element_type=jnp.float32,
        )
        + mapping_offset[:, None]
    )
    merged_sum = mapped_features.at[:, arrived_cells].add(
        arrived[:, :features].astype(jnp.float32).T, mode="drop"
    )
    merged = merged_sum.astype(jnp.bfloat16).reshape(features, north_south_total, east_west_total)

    rimmed = shifted(merged, "lon", 2, 2, True)
    rimmed = shifted(rimmed, "lat", 1, 2, False)
    hidden = jax.nn.gelu(
        conv_valid(rimmed, initial_filter_matrix) + initial_filter_offset[:, None, None]
    ).astype(jnp.bfloat16)
    lat_index = lax.axis_index("lat")
    hidden_rows = jnp.arange(north_south_total + 2)
    outside = ((hidden_rows == 0) & (lat_index == 0)) | (
        (hidden_rows == north_south_total + 1) & (lat_index == lat_size - 1)
    )
    hidden = jnp.where(outside[None, :, None], jnp.zeros_like(hidden), hidden)
    second = conv_valid(hidden, latter_filter_matrix)
    corrected = (merged.astype(jnp.float32) + second + latter_filter_offset[:, None, None]).astype(
        jnp.bfloat16
    )
    read_cell = jnp.clip(arrived_cells, 0, mesh_point_total - 1)
    picked = corrected.reshape(features, mesh_point_total)[:, read_cell].T
    returned = lax.all_to_all(
        picked.reshape(devices, capacity, features),
        ("lon", "lat"),
        split_axis=0,
        concat_axis=0,
        tiled=True,
    )
    station_values = returned.reshape(slot_total, features)[position]
    return (corrected, station_values)


def solution(mesh):
    placed = (
        P(None, "lat", "lon"),
        P(),
        P(),
        P(("lon", "lat"), None),
        P(),
        P(),
        P(("lon", "lat"), None),
        P(("lon", "lat")),
        P(),
        P(),
        P(),
        P(),
    )
    return jax.shard_map(
        on_device,
        mesh=mesh,
        in_specs=placed,
        out_specs=(P(None, "lat", "lon"), P(("lon", "lat"), None)),
        check_vma=False,
    )
```

```python
import jax
import jax.numpy as jnp
from jax import lax
from jax.sharding import PartitionSpec as P


def shifted(block, axis, dim, width, periodic):
    count = lax.axis_size(axis)
    forward = [(i, i + 1) for i in range(count - 1)]
    if periodic:
        forward.append((count - 1, 0))
    backward = [(target, source) for source, target in forward]
    low = lax.ppermute(lax.slice_in_dim(block, block.shape[dim] - width, None, axis=dim), axis, forward)
    high = lax.ppermute(lax.slice_in_dim(block, 0, width, axis=dim), axis, backward)
    return jnp.concatenate([low, block, high], axis=dim)


def conv_valid(field, kernel):
    result = lax.conv_general_dilated(
        field[None],
        kernel,
        (1, 1),
        "VALID",
        dimension_numbers=("NHWC", "OIHW", "NHWC"),
        preferred_element_type=jnp.float32,
    )
    return result[0]


def on_device(
    ensemble_prediction,
    mapping_matrix,
    mapping_offset,
    gauge_measured_records,
    gauge_scatter_matrix,
    gauge_scatter_offset,
    gauge_block_number,
    gauge_point_position,
    initial_filter_matrix,
    initial_filter_offset,
    latter_filter_matrix,
    latter_filter_offset,
):
    feature_depth_total, north_south_total, east_west_total = ensemble_prediction.shape
    features = mapping_matrix.shape[0]
    mesh_point_total = north_south_total * east_west_total
    lon_size = lax.axis_size("lon")
    lat_size = lax.axis_size("lat")
    devices = lon_size * lat_size
    held_rows = gauge_measured_records.shape[0]
    capacity = 2 * held_rows // devices
    slot_total = devices * capacity
    target_tile = gauge_block_number[:, 0]
    one_hot = (target_tile[:, None] == jnp.arange(devices, dtype=jnp.int32)[None, :]).astype(
        jnp.int32
    )
    earlier = jnp.cumsum(one_hot, axis=0) - one_hot
    slot_index = jnp.sum(earlier * one_hot, axis=1)
    position = target_tile * capacity + slot_index
    local_embedded = (
        jnp.dot(gauge_measured_records, gauge_scatter_matrix, preferred_element_type=jnp.float32)
        + gauge_scatter_offset[None, :]
    ).astype(jnp.bfloat16)
    cell_row = gauge_point_position // east_west_total
    cell_col = gauge_point_position % east_west_total
    tagged = jnp.concatenate(
        [
            local_embedded,
            (cell_row + 1).astype(jnp.bfloat16)[:, None],
            cell_col.astype(jnp.bfloat16)[:, None],
        ],
        axis=1,
    )
    width = tagged.shape[1]
    payload = jnp.zeros((slot_total, width), jnp.bfloat16).at[position].set(tagged)
    arrived = lax.all_to_all(
        payload.reshape(devices, capacity, width),
        ("lon", "lat"),
        split_axis=0,
        concat_axis=0,
        tiled=True,
    ).reshape(slot_total, width)
    arrived_row = arrived[:, features].astype(jnp.int32) - 1
    arrived_col = arrived[:, features + 1].astype(jnp.int32)
    filled = arrived_row >= 0
    arrived_cells = jnp.where(filled, arrived_row * east_west_total + arrived_col, mesh_point_total)
    mapped_features = (
        jnp.einsum(
            "krl,ck->rlc",
            ensemble_prediction,
            mapping_matrix,
            preferred_element_type=jnp.float32,
        )
        + mapping_offset
    ).reshape(mesh_point_total, features)
    merged_sum = mapped_features.at[arrived_cells].add(
        arrived[:, :features].astype(jnp.float32), mode="drop"
    )
    merged = merged_sum.astype(jnp.bfloat16).reshape(north_south_total, east_west_total, features)

    rimmed = shifted(merged, "lon", 1, 2, True)
    rimmed = shifted(rimmed, "lat", 0, 2, False)
    hidden = jax.nn.gelu(conv_valid(rimmed, initial_filter_matrix) + initial_filter_offset).astype(
        jnp.bfloat16
    )
    lat_index = lax.axis_index("lat")
    hidden_rows = jnp.arange(north_south_total + 2)
    outside = ((hidden_rows == 0) & (lat_index == 0)) | (
        (hidden_rows == north_south_total + 1) & (lat_index == lat_size - 1)
    )
    hidden = jnp.where(outside[:, None, None], jnp.zeros_like(hidden), hidden)
    second = conv_valid(hidden, latter_filter_matrix)
    corrected_cells = (merged.astype(jnp.float32) + second + latter_filter_offset).astype(jnp.bfloat16)
    corrected = jnp.transpose(corrected_cells, (2, 0, 1))
    read_cell = jnp.clip(arrived_cells, 0, mesh_point_total - 1)
    picked = corrected_cells.reshape(mesh_point_total, features)[read_cell]
    returned = lax.all_to_all(
        picked.reshape(devices, capacity, features),
        ("lon", "lat"),
        split_axis=0,
        concat_axis=0,
        tiled=True,
    )
    station_values = returned.reshape(slot_total, features)[position]
    return (corrected, station_values)


def solution(mesh):
    placed = (
        P(None, "lat", "lon"),
        P(),
        P(),
        P(("lon", "lat"), None),
        P(),
        P(),
        P(("lon", "lat"), None),
        P(("lon", "lat")),
        P(),
        P(),
        P(),
        P(),
    )
    return jax.shard_map(
        on_device,
        mesh=mesh,
        in_specs=placed,
        out_specs=(P(None, "lat", "lon"), P(("lon", "lat"), None)),
        check_vma=False,
    )
```

```python
import jax
import jax.numpy as jnp
from jax import lax
from jax.experimental import pallas as pl
from jax.experimental.pallas import tpu as pltpu
from jax.sharding import PartitionSpec as P


def whole(shape):
    return pl.BlockSpec(shape, lambda g, counts, cells: (0,) * len(shape))


def scatter_add_cells(counts, cells, base, update, capacity):
    cell_total, width = base.shape
    slot_total = update.shape[0]

    def body(counts_ref, cells_ref, base_ref, update_ref, out_ref, total_ref):
        total_ref[...] = base_ref[...]

        def source(block, carry):
            def station(rank, carry):
                slot = block * capacity + rank
                cell = cells_ref[slot]
                total_ref[pl.ds(cell, 1), :] = (
                    total_ref[pl.ds(cell, 1), :] + update_ref[pl.ds(slot, 1), :]
                )
                return carry

            return lax.fori_loop(0, counts_ref[block], station, carry)

        lax.fori_loop(0, slot_total // capacity, source, 0)
        out_ref[...] = total_ref[...].astype(out_ref.dtype)

    return pl.pallas_call(
        body,
        grid_spec=pltpu.PrefetchScalarGridSpec(
            num_scalar_prefetch=2,
            grid=(1,),
            in_specs=[whole(base.shape), whole(update.shape)],
            out_specs=whole(base.shape),
            scratch_shapes=[pltpu.VMEM(base.shape, jnp.float32)],
        ),
        out_shape=jax.ShapeDtypeStruct(base.shape, jnp.bfloat16),
        compiler_params=pltpu.CompilerParams(vmem_limit_bytes=56 * 1024 * 1024),
    )(counts, cells, base, update)


def gather_cells(counts, cells, field, capacity):
    cell_total, width = field.shape
    slot_total = cells.shape[0]

    def body(counts_ref, cells_ref, field_ref, out_ref):
        out_ref[...] = jnp.zeros(out_ref.shape, out_ref.dtype)

        def source(block, carry):
            def station(rank, carry):
                slot = block * capacity + rank
                out_ref[pl.ds(slot, 1), :] = field_ref[pl.ds(cells_ref[slot], 1), :]
                return carry

            return lax.fori_loop(0, counts_ref[block], station, carry)

        lax.fori_loop(0, slot_total // capacity, source, 0)

    return pl.pallas_call(
        body,
        grid_spec=pltpu.PrefetchScalarGridSpec(
            num_scalar_prefetch=2,
            grid=(1,),
            in_specs=[whole(field.shape)],
            out_specs=whole((slot_total, width)),
        ),
        out_shape=jax.ShapeDtypeStruct((slot_total, width), field.dtype),
        compiler_params=pltpu.CompilerParams(vmem_limit_bytes=56 * 1024 * 1024),
    )(counts, cells, field)


def shifted(block, axis, dim, width, periodic):
    count = lax.axis_size(axis)
    forward = [(i, i + 1) for i in range(count - 1)]
    if periodic:
        forward.append((count - 1, 0))
    backward = [(target, source) for source, target in forward]
    low = lax.ppermute(lax.slice_in_dim(block, block.shape[dim] - width, None, axis=dim), axis, forward)
    high = lax.ppermute(lax.slice_in_dim(block, 0, width, axis=dim), axis, backward)
    return jnp.concatenate([low, block, high], axis=dim)


def conv_valid(field, kernel):
    result = lax.conv_general_dilated(
        field[None],
        kernel,
        (1, 1),
        "VALID",
        dimension_numbers=("NHWC", "OIHW", "NHWC"),
        preferred_element_type=jnp.float32,
    )
    return result[0]


def on_device(
    ensemble_prediction,
    mapping_matrix,
    mapping_offset,
    gauge_measured_records,
    gauge_scatter_matrix,
    gauge_scatter_offset,
    gauge_block_number,
    gauge_point_position,
    initial_filter_matrix,
    initial_filter_offset,
    latter_filter_matrix,
    latter_filter_offset,
):
    feature_depth_total, north_south_total, east_west_total = ensemble_prediction.shape
    features = mapping_matrix.shape[0]
    mesh_point_total = north_south_total * east_west_total
    lon_size = lax.axis_size("lon")
    lat_size = lax.axis_size("lat")
    devices = lon_size * lat_size
    held_rows = gauge_measured_records.shape[0]
    capacity = 2 * held_rows // devices
    slot_total = devices * capacity
    target_tile = gauge_block_number[:, 0]
    one_hot = (target_tile[:, None] == jnp.arange(devices, dtype=jnp.int32)[None, :]).astype(
        jnp.int32
    )
    earlier = jnp.cumsum(one_hot, axis=0) - one_hot
    slot_index = jnp.sum(earlier * one_hot, axis=1)
    position = target_tile * capacity + slot_index
    local_embedded = (
        jnp.dot(gauge_measured_records, gauge_scatter_matrix, preferred_element_type=jnp.float32)
        + gauge_scatter_offset[None, :]
    ).astype(jnp.bfloat16)
    cell_row = gauge_point_position // east_west_total
    cell_col = gauge_point_position % east_west_total
    tagged = jnp.concatenate(
        [
            local_embedded,
            (cell_row + 1).astype(jnp.bfloat16)[:, None],
            cell_col.astype(jnp.bfloat16)[:, None],
        ],
        axis=1,
    )
    width = tagged.shape[1]
    payload = jnp.zeros((slot_total, width), jnp.bfloat16).at[position].set(tagged)
    arrived = lax.all_to_all(
        payload.reshape(devices, capacity, width),
        ("lon", "lat"),
        split_axis=0,
        concat_axis=0,
        tiled=True,
    ).reshape(slot_total, width)
    arrived_row = arrived[:, features].astype(jnp.int32) - 1
    arrived_col = arrived[:, features + 1].astype(jnp.int32)
    filled = arrived_row >= 0
    arrived_cells = jnp.where(
        filled, jnp.clip(arrived_row * east_west_total + arrived_col, 0, mesh_point_total - 1), 0
    )
    rank_of = jnp.arange(slot_total, dtype=jnp.int32) % capacity + 1
    counts = jnp.max(jnp.where(filled, rank_of, 0).reshape(devices, capacity), axis=1)
    mapped_features = (
        jnp.einsum(
            "krl,ck->rlc",
            ensemble_prediction,
            mapping_matrix,
            preferred_element_type=jnp.float32,
        )
        + mapping_offset
    ).reshape(mesh_point_total, features)
    merged = scatter_add_cells(
        counts, arrived_cells, mapped_features, arrived[:, :features].astype(jnp.float32), capacity
    ).reshape(north_south_total, east_west_total, features)

    rimmed = shifted(merged, "lon", 1, 2, True)
    rimmed = shifted(rimmed, "lat", 0, 2, False)
    hidden = jax.nn.gelu(conv_valid(rimmed, initial_filter_matrix) + initial_filter_offset).astype(
        jnp.bfloat16
    )
    lat_index = lax.axis_index("lat")
    hidden_rows = jnp.arange(north_south_total + 2)
    outside = ((hidden_rows == 0) & (lat_index == 0)) | (
        (hidden_rows == north_south_total + 1) & (lat_index == lat_size - 1)
    )
    hidden = jnp.where(outside[:, None, None], jnp.zeros_like(hidden), hidden)
    second = conv_valid(hidden, latter_filter_matrix)
    corrected_cells = (merged.astype(jnp.float32) + second + latter_filter_offset).astype(jnp.bfloat16)
    corrected = jnp.transpose(corrected_cells, (2, 0, 1))
    picked = gather_cells(
        counts,
        arrived_cells,
        corrected_cells.reshape(mesh_point_total, features).astype(jnp.float32),
        capacity,
    ).astype(jnp.bfloat16)
    returned = lax.all_to_all(
        picked.reshape(devices, capacity, features),
        ("lon", "lat"),
        split_axis=0,
        concat_axis=0,
        tiled=True,
    )
    station_values = returned.reshape(slot_total, features)[position]
    return (corrected, station_values)


def solution(mesh):
    placed = (
        P(None, "lat", "lon"),
        P(),
        P(),
        P(("lon", "lat"), None),
        P(),
        P(),
        P(("lon", "lat"), None),
        P(("lon", "lat")),
        P(),
        P(),
        P(),
        P(),
    )
    return jax.shard_map(
        on_device,
        mesh=mesh,
        in_specs=placed,
        out_specs=(P(None, "lat", "lon"), P(("lon", "lat"), None)),
        check_vma=False,
    )
```

```python
import jax
import jax.numpy as jnp
from jax import lax
from jax.sharding import PartitionSpec as P


def shifted(block, axis, dim, width, periodic):
    count = lax.axis_size(axis)
    forward = [(i, i + 1) for i in range(count - 1)]
    if periodic:
        forward.append((count - 1, 0))
    backward = [(target, source) for source, target in forward]
    low = lax.ppermute(lax.slice_in_dim(block, block.shape[dim] - width, None, axis=dim), axis, forward)
    high = lax.ppermute(lax.slice_in_dim(block, 0, width, axis=dim), axis, backward)
    return jnp.concatenate([low, block, high], axis=dim)


def conv_valid(field, kernel):
    result = lax.conv_general_dilated(
        field[None],
        kernel,
        (1, 1),
        "VALID",
        dimension_numbers=("NHWC", "OIHW", "NHWC"),
        preferred_element_type=jnp.float32,
    )
    return result[0]


def on_device(
    ensemble_prediction,
    mapping_matrix,
    mapping_offset,
    gauge_measured_records,
    gauge_scatter_matrix,
    gauge_scatter_offset,
    gauge_block_number,
    gauge_point_position,
    initial_filter_matrix,
    initial_filter_offset,
    latter_filter_matrix,
    latter_filter_offset,
):
    feature_depth_total, north_south_total, east_west_total = ensemble_prediction.shape
    features = mapping_matrix.shape[0]
    mesh_point_total = north_south_total * east_west_total
    lon_size = lax.axis_size("lon")
    lat_size = lax.axis_size("lat")
    devices = lon_size * lat_size
    held_rows = gauge_measured_records.shape[0]
    capacity = 2 * held_rows // devices
    slot_total = devices * capacity
    target_tile = gauge_block_number[:, 0]
    one_hot = (target_tile[:, None] == jnp.arange(devices, dtype=jnp.int32)[None, :]).astype(
        jnp.int32
    )
    earlier = jnp.cumsum(one_hot, axis=0) - one_hot
    slot_index = jnp.sum(earlier * one_hot, axis=1)
    position = target_tile * capacity + slot_index
    local_embedded = (
        jnp.dot(gauge_measured_records, gauge_scatter_matrix, preferred_element_type=jnp.float32)
        + gauge_scatter_offset[None, :]
    ).astype(jnp.bfloat16)
    cell_row = gauge_point_position // east_west_total
    cell_col = gauge_point_position % east_west_total
    tagged = jnp.concatenate(
        [
            local_embedded,
            (cell_row + 1).astype(jnp.bfloat16)[:, None],
            cell_col.astype(jnp.bfloat16)[:, None],
        ],
        axis=1,
    )
    width = tagged.shape[1]
    placing = (position[None, :] == jnp.arange(slot_total, dtype=jnp.int32)[:, None]).astype(
        jnp.bfloat16
    )
    payload = jnp.dot(placing, tagged, preferred_element_type=jnp.float32).astype(jnp.bfloat16)
    arrived = lax.all_to_all(
        payload.reshape(devices, capacity, width),
        ("lon", "lat"),
        split_axis=0,
        concat_axis=0,
        tiled=True,
    ).reshape(slot_total, width)
    arrived_row = arrived[:, features].astype(jnp.int32) - 1
    arrived_col = arrived[:, features + 1].astype(jnp.int32)
    filled = arrived_row >= 0
    arrived_cells = jnp.where(filled, arrived_row * east_west_total + arrived_col, mesh_point_total)
    mapped_features = (
        jnp.einsum(
            "krl,ck->rlc",
            ensemble_prediction,
            mapping_matrix,
            preferred_element_type=jnp.float32,
        )
        + mapping_offset
    ).reshape(mesh_point_total, features)
    merged_sum = mapped_features.at[arrived_cells].add(
        arrived[:, :features].astype(jnp.float32), mode="drop"
    )
    merged = merged_sum.astype(jnp.bfloat16).reshape(north_south_total, east_west_total, features)

    rimmed = shifted(merged, "lon", 1, 2, True)
    rimmed = shifted(rimmed, "lat", 0, 2, False)
    hidden = jax.nn.gelu(conv_valid(rimmed, initial_filter_matrix) + initial_filter_offset).astype(
        jnp.bfloat16
    )
    lat_index = lax.axis_index("lat")
    hidden_rows = jnp.arange(north_south_total + 2)
    outside = ((hidden_rows == 0) & (lat_index == 0)) | (
        (hidden_rows == north_south_total + 1) & (lat_index == lat_size - 1)
    )
    hidden = jnp.where(outside[:, None, None], jnp.zeros_like(hidden), hidden)
    second = conv_valid(hidden, latter_filter_matrix)
    corrected_cells = (merged.astype(jnp.float32) + second + latter_filter_offset).astype(jnp.bfloat16)
    corrected = jnp.transpose(corrected_cells, (2, 0, 1))
    read_cell = jnp.clip(arrived_cells, 0, mesh_point_total - 1)
    picked = corrected_cells.reshape(mesh_point_total, features)[read_cell]
    returned = lax.all_to_all(
        picked.reshape(devices, capacity, features),
        ("lon", "lat"),
        split_axis=0,
        concat_axis=0,
        tiled=True,
    )
    station_values = jnp.dot(
        placing.T, returned.reshape(slot_total, features), preferred_element_type=jnp.float32
    ).astype(jnp.bfloat16)
    return (corrected, station_values)


def solution(mesh):
    placed = (
        P(None, "lat", "lon"),
        P(),
        P(),
        P(("lon", "lat"), None),
        P(),
        P(),
        P(("lon", "lat"), None),
        P(("lon", "lat")),
        P(),
        P(),
        P(),
        P(),
    )
    return jax.shard_map(
        on_device,
        mesh=mesh,
        in_specs=placed,
        out_specs=(P(None, "lat", "lon"), P(("lon", "lat"), None)),
        check_vma=False,
    )
```

```python
import jax
import jax.numpy as jnp
from jax import lax
from jax.sharding import PartitionSpec as P


def shifted(block, axis, dim, width, periodic):
    count = lax.axis_size(axis)
    forward = [(i, i + 1) for i in range(count - 1)]
    if periodic:
        forward.append((count - 1, 0))
    backward = [(target, source) for source, target in forward]
    low = lax.ppermute(lax.slice_in_dim(block, block.shape[dim] - width, None, axis=dim), axis, forward)
    high = lax.ppermute(lax.slice_in_dim(block, 0, width, axis=dim), axis, backward)
    return jnp.concatenate([low, block, high], axis=dim)


def rimmed(block, width):
    lon_size = lax.axis_size("lon")
    lat_size = lax.axis_size("lat")

    def moved(piece, lon_step, lat_step):
        pairs = []
        for lon in range(lon_size):
            for lat in range(lat_size):
                to_lat = lat + lat_step
                if 0 <= to_lat < lat_size:
                    to_lon = (lon + lon_step) % lon_size
                    pairs.append((lon * lat_size + lat, to_lon * lat_size + to_lat))
        if lat_step == 0:
            return lax.ppermute(piece, "lon", [(lon, (lon + lon_step) % lon_size) for lon in range(lon_size)])
        return lax.ppermute(piece, ("lon", "lat"), pairs)

    rows, cols = block.shape[0], block.shape[1]
    first_rows, last_rows = slice(0, width), slice(rows - width, rows)
    first_cols, last_cols = slice(0, width), slice(cols - width, cols)
    every = slice(0, None)
    parts = []
    for lat_step, take_rows in ((1, last_rows), (0, every), (-1, first_rows)):
        parts.append(
            jnp.concatenate(
                [
                    moved(block[take_rows, last_cols], 1, lat_step),
                    block[take_rows, every] if lat_step == 0 else moved(block[take_rows, every], 0, lat_step),
                    moved(block[take_rows, first_cols], -1, lat_step),
                ],
                axis=1,
            )
        )
    return jnp.concatenate(parts, axis=0)


def conv_valid(field, kernel):
    result = lax.conv_general_dilated(
        field[None],
        kernel,
        (1, 1),
        "VALID",
        dimension_numbers=("NHWC", "OIHW", "NHWC"),
        preferred_element_type=jnp.float32,
    )
    return result[0]


def on_device(
    ensemble_prediction,
    mapping_matrix,
    mapping_offset,
    gauge_measured_records,
    gauge_scatter_matrix,
    gauge_scatter_offset,
    gauge_block_number,
    gauge_point_position,
    initial_filter_matrix,
    initial_filter_offset,
    latter_filter_matrix,
    latter_filter_offset,
):
    feature_depth_total, north_south_total, east_west_total = ensemble_prediction.shape
    features = mapping_matrix.shape[0]
    mesh_point_total = north_south_total * east_west_total
    lon_size = lax.axis_size("lon")
    lat_size = lax.axis_size("lat")
    devices = lon_size * lat_size
    held_rows = gauge_measured_records.shape[0]
    capacity = 2 * held_rows // devices
    slot_total = devices * capacity
    target_tile = gauge_block_number[:, 0]
    one_hot = (target_tile[:, None] == jnp.arange(devices, dtype=jnp.int32)[None, :]).astype(
        jnp.int32
    )
    earlier = jnp.cumsum(one_hot, axis=0) - one_hot
    slot_index = jnp.sum(earlier * one_hot, axis=1)
    position = target_tile * capacity + slot_index
    local_embedded = (
        jnp.dot(gauge_measured_records, gauge_scatter_matrix, preferred_element_type=jnp.float32)
        + gauge_scatter_offset[None, :]
    ).astype(jnp.bfloat16)
    cell_row = gauge_point_position // east_west_total
    cell_col = gauge_point_position % east_west_total
    tagged = jnp.concatenate(
        [
            local_embedded,
            (cell_row + 1).astype(jnp.bfloat16)[:, None],
            cell_col.astype(jnp.bfloat16)[:, None],
        ],
        axis=1,
    )
    width = tagged.shape[1]
    payload = jnp.zeros((slot_total, width), jnp.bfloat16).at[position].set(tagged)
    arrived = lax.all_to_all(
        payload.reshape(devices, capacity, width),
        ("lon", "lat"),
        split_axis=0,
        concat_axis=0,
        tiled=True,
    ).reshape(slot_total, width)
    arrived_row = arrived[:, features].astype(jnp.int32) - 1
    arrived_col = arrived[:, features + 1].astype(jnp.int32)
    filled = arrived_row >= 0
    arrived_cells = jnp.where(filled, arrived_row * east_west_total + arrived_col, mesh_point_total)
    mapped_features = (
        jnp.einsum(
            "krl,ck->rlc",
            ensemble_prediction,
            mapping_matrix,
            preferred_element_type=jnp.float32,
        )
        + mapping_offset
    ).reshape(mesh_point_total, features)
    merged_sum = mapped_features.at[arrived_cells].add(
        arrived[:, :features].astype(jnp.float32), mode="drop"
    )
    merged = merged_sum.astype(jnp.bfloat16).reshape(north_south_total, east_west_total, features)

    hidden = jax.nn.gelu(conv_valid(rimmed(merged, 2), initial_filter_matrix) + initial_filter_offset).astype(
        jnp.bfloat16
    )
    lat_index = lax.axis_index("lat")
    hidden_rows = jnp.arange(north_south_total + 2)
    outside = ((hidden_rows == 0) & (lat_index == 0)) | (
        (hidden_rows == north_south_total + 1) & (lat_index == lat_size - 1)
    )
    hidden = jnp.where(outside[:, None, None], jnp.zeros_like(hidden), hidden)
    second = conv_valid(hidden, latter_filter_matrix)
    corrected_cells = (merged.astype(jnp.float32) + second + latter_filter_offset).astype(jnp.bfloat16)
    corrected = jnp.transpose(corrected_cells, (2, 0, 1))
    read_cell = jnp.clip(arrived_cells, 0, mesh_point_total - 1)
    picked = corrected_cells.reshape(mesh_point_total, features)[read_cell]
    returned = lax.all_to_all(
        picked.reshape(devices, capacity, features),
        ("lon", "lat"),
        split_axis=0,
        concat_axis=0,
        tiled=True,
    )
    station_values = returned.reshape(slot_total, features)[position]
    return (corrected, station_values)


def solution(mesh):
    placed = (
        P(None, "lat", "lon"),
        P(),
        P(),
        P(("lon", "lat"), None),
        P(),
        P(),
        P(("lon", "lat"), None),
        P(("lon", "lat")),
        P(),
        P(),
        P(),
        P(),
    )
    return jax.shard_map(
        on_device,
        mesh=mesh,
        in_specs=placed,
        out_specs=(P(None, "lat", "lon"), P(("lon", "lat"), None)),
        check_vma=False,
    )
```

```python
import jax
import jax.numpy as jnp
from jax import lax
from jax.sharding import PartitionSpec as P


def shifted(block, axis, dim, width, periodic):
    count = lax.axis_size(axis)
    forward = [(i, i + 1) for i in range(count - 1)]
    if periodic:
        forward.append((count - 1, 0))
    backward = [(target, source) for source, target in forward]
    low = lax.ppermute(lax.slice_in_dim(block, block.shape[dim] - width, None, axis=dim), axis, forward)
    high = lax.ppermute(lax.slice_in_dim(block, 0, width, axis=dim), axis, backward)
    return jnp.concatenate([low, block, high], axis=dim)


def conv_valid(field, kernel, kind=jnp.float32):
    result = lax.conv_general_dilated(
        field[None],
        kernel,
        (1, 1),
        "VALID",
        dimension_numbers=("NHWC", "OIHW", "NHWC"),
        preferred_element_type=kind,
    )
    return result[0]


def on_device(
    ensemble_prediction,
    mapping_matrix,
    mapping_offset,
    gauge_measured_records,
    gauge_scatter_matrix,
    gauge_scatter_offset,
    gauge_block_number,
    gauge_point_position,
    initial_filter_matrix,
    initial_filter_offset,
    latter_filter_matrix,
    latter_filter_offset,
):
    feature_depth_total, north_south_total, east_west_total = ensemble_prediction.shape
    features = mapping_matrix.shape[0]
    mesh_point_total = north_south_total * east_west_total
    lon_size = lax.axis_size("lon")
    lat_size = lax.axis_size("lat")
    devices = lon_size * lat_size
    held_rows = gauge_measured_records.shape[0]
    capacity = 2 * held_rows // devices
    slot_total = devices * capacity
    target_tile = gauge_block_number[:, 0]
    one_hot = (target_tile[:, None] == jnp.arange(devices, dtype=jnp.int32)[None, :]).astype(
        jnp.int32
    )
    earlier = jnp.cumsum(one_hot, axis=0) - one_hot
    slot_index = jnp.sum(earlier * one_hot, axis=1)
    position = target_tile * capacity + slot_index
    local_embedded = (
        jnp.dot(gauge_measured_records, gauge_scatter_matrix, preferred_element_type=jnp.float32)
        + gauge_scatter_offset[None, :]
    ).astype(jnp.bfloat16)
    cell_row = gauge_point_position // east_west_total
    cell_col = gauge_point_position % east_west_total
    tagged = jnp.concatenate(
        [
            local_embedded,
            (cell_row + 1).astype(jnp.bfloat16)[:, None],
            cell_col.astype(jnp.bfloat16)[:, None],
        ],
        axis=1,
    )
    width = tagged.shape[1]
    payload = jnp.zeros((slot_total, width), jnp.bfloat16).at[position].set(tagged)
    arrived = lax.all_to_all(
        payload.reshape(devices, capacity, width),
        ("lon", "lat"),
        split_axis=0,
        concat_axis=0,
        tiled=True,
    ).reshape(slot_total, width)
    arrived_row = arrived[:, features].astype(jnp.int32) - 1
    arrived_col = arrived[:, features + 1].astype(jnp.int32)
    filled = arrived_row >= 0
    arrived_cells = jnp.where(filled, arrived_row * east_west_total + arrived_col, mesh_point_total)
    mapped_features = (
        jnp.einsum(
            "krl,ck->rlc",
            ensemble_prediction,
            mapping_matrix,
            preferred_element_type=jnp.float32,
        )
        + mapping_offset
    ).reshape(mesh_point_total, features)
    merged_sum = mapped_features.at[arrived_cells].add(
        arrived[:, :features].astype(jnp.float32), mode="drop"
    )
    merged = merged_sum.astype(jnp.bfloat16).reshape(north_south_total, east_west_total, features)

    rimmed = shifted(merged, "lon", 1, 2, True)
    rimmed = shifted(rimmed, "lat", 0, 2, False)
    hidden = jax.nn.gelu(conv_valid(rimmed, initial_filter_matrix) + initial_filter_offset).astype(
        jnp.bfloat16
    )
    lat_index = lax.axis_index("lat")
    hidden_rows = jnp.arange(north_south_total + 2)
    outside = ((hidden_rows == 0) & (lat_index == 0)) | (
        (hidden_rows == north_south_total + 1) & (lat_index == lat_size - 1)
    )
    hidden = jnp.where(outside[:, None, None], jnp.zeros_like(hidden), hidden)
    second = conv_valid(hidden, latter_filter_matrix, jnp.bfloat16)
    corrected_cells = (
        merged.astype(jnp.float32) + second.astype(jnp.float32) + latter_filter_offset
    ).astype(jnp.bfloat16)
    corrected = jnp.transpose(corrected_cells, (2, 0, 1))
    read_cell = jnp.clip(arrived_cells, 0, mesh_point_total - 1)
    picked = corrected_cells.reshape(mesh_point_total, features)[read_cell]
    returned = lax.all_to_all(
        picked.reshape(devices, capacity, features),
        ("lon", "lat"),
        split_axis=0,
        concat_axis=0,
        tiled=True,
    )
    station_values = returned.reshape(slot_total, features)[position]
    return (corrected, station_values)


def solution(mesh):
    placed = (
        P(None, "lat", "lon"),
        P(),
        P(),
        P(("lon", "lat"), None),
        P(),
        P(),
        P(("lon", "lat"), None),
        P(("lon", "lat")),
        P(),
        P(),
        P(),
        P(),
    )
    return jax.shard_map(
        on_device,
        mesh=mesh,
        in_specs=placed,
        out_specs=(P(None, "lat", "lon"), P(("lon", "lat"), None)),
        check_vma=False,
    )
```

```python
import jax
import jax.numpy as jnp
from jax import lax
from jax.sharding import PartitionSpec as P


def shifted(block, axis, dim, width, periodic):
    count = lax.axis_size(axis)
    forward = [(i, i + 1) for i in range(count - 1)]
    if periodic:
        forward.append((count - 1, 0))
    backward = [(target, source) for source, target in forward]
    low = lax.ppermute(lax.slice_in_dim(block, block.shape[dim] - width, None, axis=dim), axis, forward)
    high = lax.ppermute(lax.slice_in_dim(block, 0, width, axis=dim), axis, backward)
    return jnp.concatenate([low, block, high], axis=dim)


def conv_valid(field, kernel, kind=jnp.float32):
    result = lax.conv_general_dilated(
        field[None],
        kernel,
        (1, 1),
        "VALID",
        dimension_numbers=("NHWC", "OIHW", "NHWC"),
        preferred_element_type=kind,
    )
    return result[0]


def on_device(
    ensemble_prediction,
    mapping_matrix,
    mapping_offset,
    gauge_measured_records,
    gauge_scatter_matrix,
    gauge_scatter_offset,
    gauge_block_number,
    gauge_point_position,
    initial_filter_matrix,
    initial_filter_offset,
    latter_filter_matrix,
    latter_filter_offset,
):
    feature_depth_total, north_south_total, east_west_total = ensemble_prediction.shape
    features = mapping_matrix.shape[0]
    mesh_point_total = north_south_total * east_west_total
    lon_size = lax.axis_size("lon")
    lat_size = lax.axis_size("lat")
    devices = lon_size * lat_size
    held_rows = gauge_measured_records.shape[0]
    capacity = 2 * held_rows // devices
    slot_total = devices * capacity
    target_tile = gauge_block_number[:, 0]
    one_hot = (target_tile[:, None] == jnp.arange(devices, dtype=jnp.int32)[None, :]).astype(
        jnp.int32
    )
    earlier = jnp.cumsum(one_hot, axis=0) - one_hot
    slot_index = jnp.sum(earlier * one_hot, axis=1)
    position = target_tile * capacity + slot_index
    local_embedded = (
        jnp.dot(gauge_measured_records, gauge_scatter_matrix, preferred_element_type=jnp.float32)
        + gauge_scatter_offset[None, :]
    ).astype(jnp.bfloat16)
    cell_row = gauge_point_position // east_west_total
    cell_col = gauge_point_position % east_west_total
    tagged = jnp.concatenate(
        [
            local_embedded,
            (cell_row + 1).astype(jnp.bfloat16)[:, None],
            cell_col.astype(jnp.bfloat16)[:, None],
        ],
        axis=1,
    )
    width = tagged.shape[1]
    payload = jnp.zeros((slot_total, width), jnp.bfloat16).at[position].set(tagged)
    arrived = lax.all_to_all(
        payload.reshape(devices, capacity, width),
        ("lon", "lat"),
        split_axis=0,
        concat_axis=0,
        tiled=True,
    ).reshape(slot_total, width)
    arrived_row = arrived[:, features].astype(jnp.int32) - 1
    arrived_col = arrived[:, features + 1].astype(jnp.int32)
    filled = arrived_row >= 0
    arrived_cells = jnp.where(filled, arrived_row * east_west_total + arrived_col, mesh_point_total)
    mapped_features = (
        jnp.einsum(
            "krl,ck->rlc",
            ensemble_prediction,
            mapping_matrix,
            preferred_element_type=jnp.float32,
        )
        + mapping_offset
    ).reshape(mesh_point_total, features)
    merged_sum = mapped_features.at[arrived_cells].add(
        arrived[:, :features].astype(jnp.float32), mode="drop"
    )
    merged = merged_sum.astype(jnp.bfloat16).reshape(north_south_total, east_west_total, features)

    rimmed = shifted(merged, "lon", 1, 2, True)
    rimmed = shifted(rimmed, "lat", 0, 2, False)
    hidden = jax.nn.gelu(conv_valid(rimmed, initial_filter_matrix) + initial_filter_offset).astype(
        jnp.bfloat16
    )
    lat_index = lax.axis_index("lat")
    hidden_rows = jnp.arange(north_south_total + 2)
    outside = ((hidden_rows == 0) & (lat_index == 0)) | (
        (hidden_rows == north_south_total + 1) & (lat_index == lat_size - 1)
    )
    hidden = jnp.where(outside[:, None, None], jnp.zeros_like(hidden), hidden)
    second = conv_valid(hidden, latter_filter_matrix, jnp.bfloat16)
    corrected_cells = (
        (merged + second).astype(jnp.float32) + latter_filter_offset
    ).astype(jnp.bfloat16)
    corrected = jnp.transpose(corrected_cells, (2, 0, 1))
    read_cell = jnp.clip(arrived_cells, 0, mesh_point_total - 1)
    picked = corrected_cells.reshape(mesh_point_total, features)[read_cell]
    returned = lax.all_to_all(
        picked.reshape(devices, capacity, features),
        ("lon", "lat"),
        split_axis=0,
        concat_axis=0,
        tiled=True,
    )
    station_values = returned.reshape(slot_total, features)[position]
    return (corrected, station_values)


def solution(mesh):
    placed = (
        P(None, "lat", "lon"),
        P(),
        P(),
        P(("lon", "lat"), None),
        P(),
        P(),
        P(("lon", "lat"), None),
        P(("lon", "lat")),
        P(),
        P(),
        P(),
        P(),
    )
    return jax.shard_map(
        on_device,
        mesh=mesh,
        in_specs=placed,
        out_specs=(P(None, "lat", "lon"), P(("lon", "lat"), None)),
        check_vma=False,
    )
```

```python
import jax
import jax.numpy as jnp
from jax import lax
from jax.sharding import PartitionSpec as P


def conv_valid(field, kernel, kind=jnp.float32):
    result = lax.conv_general_dilated(
        field[None],
        kernel,
        (1, 1),
        "VALID",
        dimension_numbers=("NHWC", "OIHW", "NHWC"),
        preferred_element_type=kind,
    )
    return result[0]


def on_device(
    ensemble_prediction,
    mapping_matrix,
    mapping_offset,
    gauge_measured_records,
    gauge_scatter_matrix,
    gauge_scatter_offset,
    gauge_block_number,
    gauge_point_position,
    initial_filter_matrix,
    initial_filter_offset,
    latter_filter_matrix,
    latter_filter_offset,
):
    feature_depth_total, north_south_total, east_west_total = ensemble_prediction.shape
    features = mapping_matrix.shape[0]
    mesh_point_total = north_south_total * east_west_total
    lon_size = lax.axis_size("lon")
    lat_size = lax.axis_size("lat")
    devices = lon_size * lat_size
    held_rows = gauge_measured_records.shape[0]
    capacity = 2 * held_rows // devices
    slot_total = devices * capacity
    target_tile = gauge_block_number[:, 0]
    one_hot = (target_tile[:, None] == jnp.arange(devices, dtype=jnp.int32)[None, :]).astype(
        jnp.int32
    )
    earlier = jnp.cumsum(one_hot, axis=0) - one_hot
    slot_index = jnp.sum(earlier * one_hot, axis=1)
    position = target_tile * capacity + slot_index
    local_embedded = (
        jnp.dot(gauge_measured_records, gauge_scatter_matrix, preferred_element_type=jnp.float32)
        + gauge_scatter_offset[None, :]
    ).astype(jnp.bfloat16)
    cell_row = gauge_point_position // east_west_total
    cell_col = gauge_point_position % east_west_total
    tagged = jnp.concatenate(
        [
            local_embedded,
            (cell_row + 1).astype(jnp.bfloat16)[:, None],
            cell_col.astype(jnp.bfloat16)[:, None],
        ],
        axis=1,
    )
    width = tagged.shape[1]
    payload = jnp.zeros((slot_total, width), jnp.bfloat16).at[position].set(tagged)
    arrived = lax.all_to_all(
        payload.reshape(devices, capacity, width),
        ("lon", "lat"),
        split_axis=0,
        concat_axis=0,
        tiled=True,
    ).reshape(slot_total, width)
    arrived_row = arrived[:, features].astype(jnp.int32) - 1
    arrived_col = arrived[:, features + 1].astype(jnp.int32)
    filled = arrived_row >= 0
    arrived_cells = jnp.where(filled, arrived_row * east_west_total + arrived_col, mesh_point_total)
    mapped_features = (
        jnp.einsum(
            "krl,ck->rlc",
            ensemble_prediction,
            mapping_matrix,
            preferred_element_type=jnp.float32,
        )
        + mapping_offset
    ).reshape(mesh_point_total, features)
    merged_sum = mapped_features.at[arrived_cells].add(
        arrived[:, :features].astype(jnp.float32), mode="drop"
    )
    merged = merged_sum.astype(jnp.bfloat16).reshape(north_south_total, east_west_total, features)

    lon_size = lax.axis_size("lon")
    lon_forward = [(i, (i + 1) % lon_size) for i in range(lon_size)]
    lon_backward = [(j, i) for i, j in lon_forward]
    lat_forward = [(i, i + 1) for i in range(lat_size - 1)]
    lat_backward = [(j, i) for i, j in lat_forward]
    west = lax.ppermute(merged[:, -2:], "lon", lon_forward)
    east = lax.ppermute(merged[:, :2], "lon", lon_backward)
    last_strip = jnp.concatenate([west[-2:], merged[-2:], east[-2:]], axis=1)
    first_strip = jnp.concatenate([west[:2], merged[:2], east[:2]], axis=1)
    north = lax.ppermute(last_strip, "lat", lat_forward)
    south = lax.ppermute(first_strip, "lat", lat_backward)
    rimmed = jnp.concatenate(
        [north, jnp.concatenate([west, merged, east], axis=1), south], axis=0
    )
    hidden = jax.nn.gelu(conv_valid(rimmed, initial_filter_matrix) + initial_filter_offset).astype(
        jnp.bfloat16
    )
    lat_index = lax.axis_index("lat")
    hidden_rows = jnp.arange(north_south_total + 2)
    outside = ((hidden_rows == 0) & (lat_index == 0)) | (
        (hidden_rows == north_south_total + 1) & (lat_index == lat_size - 1)
    )
    hidden = jnp.where(outside[:, None, None], jnp.zeros_like(hidden), hidden)
    second = conv_valid(hidden, latter_filter_matrix, jnp.bfloat16)
    corrected_cells = (
        (merged + second).astype(jnp.float32) + latter_filter_offset
    ).astype(jnp.bfloat16)
    corrected = jnp.transpose(corrected_cells, (2, 0, 1))
    read_cell = jnp.clip(arrived_cells, 0, mesh_point_total - 1)
    picked = corrected_cells.reshape(mesh_point_total, features)[read_cell]
    returned = lax.all_to_all(
        picked.reshape(devices, capacity, features),
        ("lon", "lat"),
        split_axis=0,
        concat_axis=0,
        tiled=True,
    )
    station_values = returned.reshape(slot_total, features)[position]
    return (corrected, station_values)


def solution(mesh):
    placed = (
        P(None, "lat", "lon"),
        P(),
        P(),
        P(("lon", "lat"), None),
        P(),
        P(),
        P(("lon", "lat"), None),
        P(("lon", "lat")),
        P(),
        P(),
        P(),
        P(),
    )
    return jax.shard_map(
        on_device,
        mesh=mesh,
        in_specs=placed,
        out_specs=(P(None, "lat", "lon"), P(("lon", "lat"), None)),
        check_vma=False,
    )
```

```python
import jax
import jax.numpy as jnp
from jax import lax
from jax.sharding import PartitionSpec as P


def shifted(block, axis, dim, width, periodic):
    count = lax.axis_size(axis)
    forward = [(i, i + 1) for i in range(count - 1)]
    if periodic:
        forward.append((count - 1, 0))
    backward = [(target, source) for source, target in forward]
    low = lax.ppermute(lax.slice_in_dim(block, block.shape[dim] - width, None, axis=dim), axis, forward)
    high = lax.ppermute(lax.slice_in_dim(block, 0, width, axis=dim), axis, backward)
    return jnp.concatenate([low, block, high], axis=dim)


def conv_valid(field, kernel, kind=jnp.float32):
    result = lax.conv_general_dilated(
        field[None],
        kernel,
        (1, 1),
        "VALID",
        dimension_numbers=("NHWC", "OIHW", "NHWC"),
        preferred_element_type=kind,
    )
    return result[0]


def on_device(
    ensemble_prediction,
    mapping_matrix,
    mapping_offset,
    gauge_measured_records,
    gauge_scatter_matrix,
    gauge_scatter_offset,
    gauge_block_number,
    gauge_point_position,
    initial_filter_matrix,
    initial_filter_offset,
    latter_filter_matrix,
    latter_filter_offset,
):
    feature_depth_total, north_south_total, east_west_total = ensemble_prediction.shape
    features = mapping_matrix.shape[0]
    mesh_point_total = north_south_total * east_west_total
    lon_size = lax.axis_size("lon")
    lat_size = lax.axis_size("lat")
    devices = lon_size * lat_size
    held_rows = gauge_measured_records.shape[0]
    capacity = 2 * held_rows // devices
    slot_total = devices * capacity
    target_tile = gauge_block_number[:, 0]
    one_hot = (target_tile[:, None] == jnp.arange(devices, dtype=jnp.int32)[None, :]).astype(
        jnp.int32
    )
    earlier = jnp.cumsum(one_hot, axis=0) - one_hot
    slot_index = jnp.sum(earlier * one_hot, axis=1)
    position = target_tile * capacity + slot_index
    local_embedded = (
        jnp.dot(gauge_measured_records, gauge_scatter_matrix, preferred_element_type=jnp.float32)
        + gauge_scatter_offset[None, :]
    ).astype(jnp.bfloat16)
    cell_row = gauge_point_position // east_west_total
    cell_col = gauge_point_position % east_west_total
    tagged = jnp.concatenate(
        [
            local_embedded,
            (cell_row + 1).astype(jnp.bfloat16)[:, None],
            cell_col.astype(jnp.bfloat16)[:, None],
        ],
        axis=1,
    )
    width = tagged.shape[1]
    payload = jnp.zeros((slot_total, width), jnp.bfloat16).at[position].set(tagged)
    arrived = lax.all_to_all(
        payload.reshape(devices, capacity, width),
        ("lon", "lat"),
        split_axis=0,
        concat_axis=0,
        tiled=True,
    ).reshape(slot_total, width)
    arrived_row = arrived[:, features].astype(jnp.int32) - 1
    arrived_col = arrived[:, features + 1].astype(jnp.int32)
    arrived_cells = jnp.clip(arrived_row * east_west_total + arrived_col, 0, mesh_point_total - 1)
    mapped_features = (
        jnp.einsum(
            "krl,ck->rlc",
            ensemble_prediction,
            mapping_matrix,
            preferred_element_type=jnp.float32,
        )
        + mapping_offset
    ).reshape(mesh_point_total, features)
    merged_sum = mapped_features.at[arrived_cells].add(
        arrived[:, :features].astype(jnp.float32), mode="promise_in_bounds"
    )
    merged = merged_sum.astype(jnp.bfloat16).reshape(north_south_total, east_west_total, features)

    rimmed = shifted(merged, "lon", 1, 2, True)
    rimmed = shifted(rimmed, "lat", 0, 2, False)
    hidden = jax.nn.gelu(conv_valid(rimmed, initial_filter_matrix) + initial_filter_offset).astype(
        jnp.bfloat16
    )
    lat_index = lax.axis_index("lat")
    hidden_rows = jnp.arange(north_south_total + 2)
    outside = ((hidden_rows == 0) & (lat_index == 0)) | (
        (hidden_rows == north_south_total + 1) & (lat_index == lat_size - 1)
    )
    hidden = jnp.where(outside[:, None, None], jnp.zeros_like(hidden), hidden)
    second = conv_valid(hidden, latter_filter_matrix, jnp.bfloat16)
    corrected_cells = (
        (merged + second).astype(jnp.float32) + latter_filter_offset
    ).astype(jnp.bfloat16)
    corrected = jnp.transpose(corrected_cells, (2, 0, 1))
    picked = corrected_cells.reshape(mesh_point_total, features).at[arrived_cells].get(
        mode="promise_in_bounds"
    )
    returned = lax.all_to_all(
        picked.reshape(devices, capacity, features),
        ("lon", "lat"),
        split_axis=0,
        concat_axis=0,
        tiled=True,
    )
    station_values = returned.reshape(slot_total, features)[position]
    return (corrected, station_values)


def solution(mesh):
    placed = (
        P(None, "lat", "lon"),
        P(),
        P(),
        P(("lon", "lat"), None),
        P(),
        P(),
        P(("lon", "lat"), None),
        P(("lon", "lat")),
        P(),
        P(),
        P(),
        P(),
    )
    return jax.shard_map(
        on_device,
        mesh=mesh,
        in_specs=placed,
        out_specs=(P(None, "lat", "lon"), P(("lon", "lat"), None)),
        check_vma=False,
    )
```

```python
import jax
import jax.numpy as jnp
from jax import lax
from jax.sharding import PartitionSpec as P


def shifted(block, axis, dim, width, periodic):
    count = lax.axis_size(axis)
    forward = [(i, i + 1) for i in range(count - 1)]
    if periodic:
        forward.append((count - 1, 0))
    backward = [(target, source) for source, target in forward]
    low = lax.ppermute(lax.slice_in_dim(block, block.shape[dim] - width, None, axis=dim), axis, forward)
    high = lax.ppermute(lax.slice_in_dim(block, 0, width, axis=dim), axis, backward)
    return jnp.concatenate([low, block, high], axis=dim)


def conv_valid(field, kernel, kind=jnp.float32):
    result = lax.conv_general_dilated(
        field[None],
        kernel,
        (1, 1),
        "VALID",
        dimension_numbers=("NHWC", "OIHW", "NHWC"),
        preferred_element_type=kind,
    )
    return result[0]


def on_device(
    ensemble_prediction,
    mapping_matrix,
    mapping_offset,
    gauge_measured_records,
    gauge_scatter_matrix,
    gauge_scatter_offset,
    gauge_block_number,
    gauge_point_position,
    initial_filter_matrix,
    initial_filter_offset,
    latter_filter_matrix,
    latter_filter_offset,
):
    feature_depth_total, north_south_total, east_west_total = ensemble_prediction.shape
    features = mapping_matrix.shape[0]
    mesh_point_total = north_south_total * east_west_total
    lon_size = lax.axis_size("lon")
    lat_size = lax.axis_size("lat")
    devices = lon_size * lat_size
    held_rows = gauge_measured_records.shape[0]
    capacity = 2 * held_rows // devices
    slot_total = devices * capacity
    target_tile = gauge_block_number[:, 0]
    one_hot = (target_tile[:, None] == jnp.arange(devices, dtype=jnp.int32)[None, :]).astype(
        jnp.int32
    )
    earlier = jnp.cumsum(one_hot, axis=0) - one_hot
    slot_index = jnp.sum(earlier * one_hot, axis=1)
    position = target_tile * capacity + slot_index
    local_embedded = (
        jnp.dot(gauge_measured_records, gauge_scatter_matrix, preferred_element_type=jnp.float32)
        + gauge_scatter_offset[None, :]
    ).astype(jnp.bfloat16)
    cell_row = gauge_point_position // east_west_total
    cell_col = gauge_point_position % east_west_total
    tagged = jnp.concatenate(
        [
            local_embedded,
            (cell_row + 1).astype(jnp.bfloat16)[:, None],
            cell_col.astype(jnp.bfloat16)[:, None],
        ],
        axis=1,
    )
    width = tagged.shape[1]
    payload = jnp.zeros((slot_total, width), jnp.bfloat16).at[position].set(tagged)
    arrived = lax.all_to_all(
        payload.reshape(devices, capacity, width),
        ("lon", "lat"),
        split_axis=0,
        concat_axis=0,
        tiled=True,
    ).reshape(slot_total, width)
    arrived_row = arrived[:, features].astype(jnp.int32) - 1
    arrived_col = arrived[:, features + 1].astype(jnp.int32)
    filled = arrived_row >= 0
    arrived_cells = jnp.where(filled, arrived_row * east_west_total + arrived_col, mesh_point_total)
    mapped_features = (
        jnp.einsum(
            "krl,ck->rlc",
            ensemble_prediction,
            mapping_matrix,
            preferred_element_type=jnp.float32,
        )
        + mapping_offset
    ).reshape(mesh_point_total, features)
    merged_sum = mapped_features.at[arrived_cells].add(
        arrived[:, :features].astype(jnp.float32), mode="drop"
    )
    merged = merged_sum.astype(jnp.bfloat16).reshape(north_south_total, east_west_total, features)

    rimmed = shifted(merged, "lon", 1, 2, True)
    rimmed = shifted(rimmed, "lat", 0, 2, False)
    hidden = jax.nn.gelu(conv_valid(rimmed, initial_filter_matrix) + initial_filter_offset).astype(
        jnp.bfloat16
    )
    lat_index = lax.axis_index("lat")
    hidden_rows = jnp.arange(north_south_total + 2)
    outside = ((hidden_rows == 0) & (lat_index == 0)) | (
        (hidden_rows == north_south_total + 1) & (lat_index == lat_size - 1)
    )
    hidden = jnp.where(outside[:, None, None], jnp.zeros_like(hidden), hidden)
    second = conv_valid(hidden, latter_filter_matrix, jnp.bfloat16)
    corrected_cells = (
        (merged + second).astype(jnp.float32) + latter_filter_offset
    ).astype(jnp.bfloat16)
    corrected = jnp.transpose(corrected_cells, (2, 0, 1))
    picked = corrected_cells.reshape(mesh_point_total, features).at[arrived_cells].get(
        mode="fill", fill_value=0
    )
    returned = lax.all_to_all(
        picked.reshape(devices, capacity, features),
        ("lon", "lat"),
        split_axis=0,
        concat_axis=0,
        tiled=True,
    )
    station_values = returned.reshape(slot_total, features)[position]
    return (corrected, station_values)


def solution(mesh):
    placed = (
        P(None, "lat", "lon"),
        P(),
        P(),
        P(("lon", "lat"), None),
        P(),
        P(),
        P(("lon", "lat"), None),
        P(("lon", "lat")),
        P(),
        P(),
        P(),
        P(),
    )
    return jax.shard_map(
        on_device,
        mesh=mesh,
        in_specs=placed,
        out_specs=(P(None, "lat", "lon"), P(("lon", "lat"), None)),
        check_vma=False,
    )
```

```python
import jax
import jax.numpy as jnp
from jax import lax
from jax.sharding import PartitionSpec as P


def shifted(block, axis, dim, width, periodic):
    count = lax.axis_size(axis)
    forward = [(i, i + 1) for i in range(count - 1)]
    if periodic:
        forward.append((count - 1, 0))
    backward = [(target, source) for source, target in forward]
    low = lax.ppermute(lax.slice_in_dim(block, block.shape[dim] - width, None, axis=dim), axis, forward)
    high = lax.ppermute(lax.slice_in_dim(block, 0, width, axis=dim), axis, backward)
    return jnp.concatenate([low, block, high], axis=dim)


def conv_valid(field, kernel, kind=jnp.float32):
    result = lax.conv_general_dilated(
        field[None],
        kernel,
        (1, 1),
        "VALID",
        dimension_numbers=("NHWC", "OIHW", "NHWC"),
        preferred_element_type=kind,
    )
    return result[0]


def on_device(
    ensemble_prediction,
    mapping_matrix,
    mapping_offset,
    gauge_measured_records,
    gauge_scatter_matrix,
    gauge_scatter_offset,
    gauge_block_number,
    gauge_point_position,
    initial_filter_matrix,
    initial_filter_offset,
    latter_filter_matrix,
    latter_filter_offset,
):
    feature_depth_total, north_south_total, east_west_total = ensemble_prediction.shape
    features = mapping_matrix.shape[0]
    mesh_point_total = north_south_total * east_west_total
    lon_size = lax.axis_size("lon")
    lat_size = lax.axis_size("lat")
    devices = lon_size * lat_size
    held_rows = gauge_measured_records.shape[0]
    capacity = 2 * held_rows // devices
    slot_total = devices * capacity
    target_tile = gauge_block_number[:, 0]
    one_hot = (target_tile[:, None] == jnp.arange(devices, dtype=jnp.int32)[None, :]).astype(
        jnp.int32
    )
    earlier = jnp.cumsum(one_hot, axis=0) - one_hot
    slot_index = jnp.sum(earlier * one_hot, axis=1)
    position = target_tile * capacity + slot_index
    local_embedded = (
        jnp.dot(gauge_measured_records, gauge_scatter_matrix, preferred_element_type=jnp.float32)
        + gauge_scatter_offset[None, :]
    ).astype(jnp.bfloat16)
    cell_row = gauge_point_position // east_west_total
    cell_col = gauge_point_position % east_west_total
    tagged = jnp.concatenate(
        [
            local_embedded,
            (cell_row + 1).astype(jnp.bfloat16)[:, None],
            cell_col.astype(jnp.bfloat16)[:, None],
        ],
        axis=1,
    )
    width = tagged.shape[1]
    payload = jnp.zeros((slot_total, width), jnp.bfloat16).at[position].set(tagged)
    arrived = lax.all_to_all(
        payload.reshape(devices, capacity, width),
        ("lon", "lat"),
        split_axis=0,
        concat_axis=0,
        tiled=True,
    ).reshape(slot_total, width)
    arrived_row = arrived[:, features].astype(jnp.int32) - 1
    arrived_col = arrived[:, features + 1].astype(jnp.int32)
    filled = arrived_row >= 0
    arrived_cells = jnp.where(filled, arrived_row * east_west_total + arrived_col, mesh_point_total)
    mapped_features = (
        jnp.einsum(
            "krl,ck->rlc",
            ensemble_prediction,
            mapping_matrix,
            preferred_element_type=jnp.float32,
        )
        + mapping_offset
    ).reshape(mesh_point_total, features)
    merged_sum = mapped_features.at[arrived_cells].add(
        arrived[:, :features].astype(jnp.float32), mode="drop"
    )
    merged_wide = merged_sum.reshape(north_south_total, east_west_total, features)
    merged = merged_wide.astype(jnp.bfloat16)

    rimmed = shifted(merged_wide, "lon", 1, 2, True)
    rimmed = shifted(rimmed, "lat", 0, 2, False).astype(jnp.bfloat16)
    hidden = jax.nn.gelu(conv_valid(rimmed, initial_filter_matrix) + initial_filter_offset).astype(
        jnp.bfloat16
    )
    lat_index = lax.axis_index("lat")
    hidden_rows = jnp.arange(north_south_total + 2)
    outside = ((hidden_rows == 0) & (lat_index == 0)) | (
        (hidden_rows == north_south_total + 1) & (lat_index == lat_size - 1)
    )
    hidden = jnp.where(outside[:, None, None], jnp.zeros_like(hidden), hidden)
    second = conv_valid(hidden, latter_filter_matrix, jnp.bfloat16)
    corrected_cells = (
        (merged + second).astype(jnp.float32) + latter_filter_offset
    ).astype(jnp.bfloat16)
    corrected = jnp.transpose(corrected_cells, (2, 0, 1))
    read_cell = jnp.clip(arrived_cells, 0, mesh_point_total - 1)
    picked = corrected_cells.reshape(mesh_point_total, features)[read_cell]
    returned = lax.all_to_all(
        picked.reshape(devices, capacity, features),
        ("lon", "lat"),
        split_axis=0,
        concat_axis=0,
        tiled=True,
    )
    station_values = returned.reshape(slot_total, features)[position]
    return (corrected, station_values)


def solution(mesh):
    placed = (
        P(None, "lat", "lon"),
        P(),
        P(),
        P(("lon", "lat"), None),
        P(),
        P(),
        P(("lon", "lat"), None),
        P(("lon", "lat")),
        P(),
        P(),
        P(),
        P(),
    )
    return jax.shard_map(
        on_device,
        mesh=mesh,
        in_specs=placed,
        out_specs=(P(None, "lat", "lon"), P(("lon", "lat"), None)),
        check_vma=False,
    )
```

```python
import jax
import jax.numpy as jnp
from jax import lax
from jax.sharding import PartitionSpec as P


def shifted(block, axis, dim, width, periodic):
    count = lax.axis_size(axis)
    forward = [(i, i + 1) for i in range(count - 1)]
    if periodic:
        forward.append((count - 1, 0))
    backward = [(target, source) for source, target in forward]
    low = lax.ppermute(lax.slice_in_dim(block, block.shape[dim] - width, None, axis=dim), axis, forward)
    high = lax.ppermute(lax.slice_in_dim(block, 0, width, axis=dim), axis, backward)
    return jnp.concatenate([low, block, high], axis=dim)


def conv_valid(field, kernel, kind=jnp.float32):
    result = lax.conv_general_dilated(
        field[None],
        kernel,
        (1, 1),
        "VALID",
        dimension_numbers=("NHWC", "OIHW", "NHWC"),
        preferred_element_type=kind,
    )
    return result[0]


def on_device(
    ensemble_prediction,
    mapping_matrix,
    mapping_offset,
    gauge_measured_records,
    gauge_scatter_matrix,
    gauge_scatter_offset,
    gauge_block_number,
    gauge_point_position,
    initial_filter_matrix,
    initial_filter_offset,
    latter_filter_matrix,
    latter_filter_offset,
):
    feature_depth_total, north_south_total, east_west_total = ensemble_prediction.shape
    features = mapping_matrix.shape[0]
    mesh_point_total = north_south_total * east_west_total
    lon_size = lax.axis_size("lon")
    lat_size = lax.axis_size("lat")
    devices = lon_size * lat_size
    held_rows = gauge_measured_records.shape[0]
    capacity = 2 * held_rows // devices
    slot_total = devices * capacity
    target_tile = gauge_block_number[:, 0]
    naming = target_tile[:, None] == jnp.arange(devices, dtype=jnp.int32)[None, :]
    span = 64 if held_rows % 64 == 0 else held_rows
    blocks = naming.astype(jnp.bfloat16).reshape(held_rows // span, span, devices)
    before = (jnp.arange(span)[:, None] > jnp.arange(span)[None, :]).astype(jnp.bfloat16)
    inside = jnp.einsum("ij,bjd->bid", before, blocks, preferred_element_type=jnp.float32)
    block_total = jnp.sum(blocks.astype(jnp.int32), axis=1)
    block_start = jnp.cumsum(block_total, axis=0) - block_total
    earlier = (inside.astype(jnp.int32) + block_start[:, None, :]).reshape(held_rows, devices)
    slot_index = jnp.sum(jnp.where(naming, earlier, 0), axis=1)
    position = target_tile * capacity + slot_index
    local_embedded = (
        jnp.dot(gauge_measured_records, gauge_scatter_matrix, preferred_element_type=jnp.float32)
        + gauge_scatter_offset[None, :]
    ).astype(jnp.bfloat16)
    cell_row = gauge_point_position // east_west_total
    cell_col = gauge_point_position % east_west_total
    tagged = jnp.concatenate(
        [
            local_embedded,
            (cell_row + 1).astype(jnp.bfloat16)[:, None],
            cell_col.astype(jnp.bfloat16)[:, None],
        ],
        axis=1,
    )
    width = tagged.shape[1]
    payload = jnp.zeros((slot_total, width), jnp.bfloat16).at[position].set(tagged)
    arrived = lax.all_to_all(
        payload.reshape(devices, capacity, width),
        ("lon", "lat"),
        split_axis=0,
        concat_axis=0,
        tiled=True,
    ).reshape(slot_total, width)
    arrived_row = arrived[:, features].astype(jnp.int32) - 1
    arrived_col = arrived[:, features + 1].astype(jnp.int32)
    filled = arrived_row >= 0
    arrived_cells = jnp.where(filled, arrived_row * east_west_total + arrived_col, mesh_point_total)
    mapped_features = (
        jnp.einsum(
            "krl,ck->rlc",
            ensemble_prediction,
            mapping_matrix,
            preferred_element_type=jnp.float32,
        )
        + mapping_offset
    ).reshape(mesh_point_total, features)
    merged_sum = mapped_features.at[arrived_cells].add(
        arrived[:, :features].astype(jnp.float32), mode="drop"
    )
    merged = merged_sum.astype(jnp.bfloat16).reshape(north_south_total, east_west_total, features)

    rimmed = shifted(merged, "lon", 1, 2, True)
    rimmed = shifted(rimmed, "lat", 0, 2, False)
    hidden = jax.nn.gelu(conv_valid(rimmed, initial_filter_matrix) + initial_filter_offset).astype(
        jnp.bfloat16
    )
    lat_index = lax.axis_index("lat")
    hidden_rows = jnp.arange(north_south_total + 2)
    outside = ((hidden_rows == 0) & (lat_index == 0)) | (
        (hidden_rows == north_south_total + 1) & (lat_index == lat_size - 1)
    )
    hidden = jnp.where(outside[:, None, None], jnp.zeros_like(hidden), hidden)
    second = conv_valid(hidden, latter_filter_matrix, jnp.bfloat16)
    corrected_cells = (
        (merged + second).astype(jnp.float32) + latter_filter_offset
    ).astype(jnp.bfloat16)
    corrected = jnp.transpose(corrected_cells, (2, 0, 1))
    read_cell = jnp.clip(arrived_cells, 0, mesh_point_total - 1)
    picked = corrected_cells.reshape(mesh_point_total, features)[read_cell]
    returned = lax.all_to_all(
        picked.reshape(devices, capacity, features),
        ("lon", "lat"),
        split_axis=0,
        concat_axis=0,
        tiled=True,
    )
    station_values = returned.reshape(slot_total, features)[position]
    return (corrected, station_values)


def solution(mesh):
    placed = (
        P(None, "lat", "lon"),
        P(),
        P(),
        P(("lon", "lat"), None),
        P(),
        P(),
        P(("lon", "lat"), None),
        P(("lon", "lat")),
        P(),
        P(),
        P(),
        P(),
    )
    return jax.shard_map(
        on_device,
        mesh=mesh,
        in_specs=placed,
        out_specs=(P(None, "lat", "lon"), P(("lon", "lat"), None)),
        check_vma=False,
    )
```
